512 devices in a mesh: dp: 128 (over z, y, core), proto: 4 (over x).
Axes of the slice: x: 4, y: 8, z: 8, core: 2. Of those that a mesh axis runs over, the one named last changes fastest.
Arguments:
- teacher_emb: bfloat16 [32768, 128], P('dp'), may hold values from -64 to 64
- student_emb: bfloat16 [32768, 128], P('dp'), may hold values from -64 to 64
- prototypes: float32 [32768, 128], P(('dp', 'proto')), may hold values from -0.125 to 0.125
Outputs:
- grad_prototypes: float32 [32768, 128], P(('dp', 'proto'))
- grad_student: float32 [32768, 128], P('dp')
The draws below stay inside these ranges and needn't reach their ends.
All inputs are finite; a program needn't handle non-finite values.
Results may differ from the reference program's by a relative error of at most 0.012.
The reference program's roundings to bfloat16 on the way (of `copies` and `grad_logits`) count: a program that leaves them out, or rounds other values in their place, can miss the bound.
Values may be sent and summed in bfloat16 or wider, within the bound.
No kernel may reach another device: no remote copies, remote signals or barrier semaphores. Data moves between devices by JAX's collectives and lax.ppermute only.
A program may use at most 64 MiB of HBM per device.

```python
import math
import jax
import jax.numpy as jnp
from jax import lax

D = 128
K = 32768
ROWS_DEV = 256
ITERS = 3
N_DP = 128


def draw_table(key):
    width_scale = 0.3 / math.sqrt(D)
    table_key = jax.random.fold_in(key, 101)
    table = jax.random.normal(table_key, (K, D), jnp.float32) * width_scale
    table = jnp.clip(table, -0.125, 0.125)
    return table


def draw_embeddings(key, salt):
    rows_total = ROWS_DEV * N_DP
    own_key = jax.random.fold_in(key, salt)
    values = jnp.clip(jax.random.normal(jax.random.fold_in(own_key, 2), (rows_total, D), jnp.float32), -6.0, 6.0)
    return jnp.clip(values, -64.0, 64.0)


def draw_teacher_emb(key, part):
    return draw_embeddings(key, 201).astype(jnp.bfloat16)


def draw_student_emb(key, part):
    return draw_embeddings(key, 301).astype(jnp.bfloat16)


def draw_prototypes(key, part):
    return draw_table(key)


def setup_inputs(seed: int = 0) -> dict:
    splits = jax.random.split(jax.random.key(seed), 4)
    return {
        "teacher_emb": draw_teacher_emb(jax.random.fold_in(splits[3], 71), 0),
        "student_emb": draw_student_emb(jax.random.fold_in(splits[3], 71), 0),
        "prototypes": draw_prototypes(jax.random.fold_in(splits[3], 71), 0),
    }


teacher_temp = 0.07
student_temp = 0.1


def contract_rows(left, right):
    return lax.dot_general(left, right, (((1,), (1,)), ((), ())), preferred_element_type=jnp.float32)


def reference(teacher_emb, student_emb, prototypes):
    copies = prototypes.astype(jnp.bfloat16)
    rows_total = teacher_emb.shape[0]
    width = teacher_emb.shape[1]
    block = math.gcd(rows_total, 1024)
    count_blocks = rows_total // block

    def teacher_block(emb):
        logits = contract_rows(emb, copies)
        top = jnp.max(logits, axis=1, keepdims=True)
        return jnp.exp((logits - top) / teacher_temp)

    base = lax.map(teacher_block, teacher_emb.reshape(count_blocks, block, width))
    base = base.reshape(rows_total, -1)
    row_scale = jnp.ones((rows_total,), jnp.float32)
    col_scale = jnp.ones((base.shape[1],), jnp.float32)
    for step in range(ITERS):
        col_scale = 1.0 / jnp.dot(row_scale, base, precision=lax.Precision.HIGHEST)
        row_scale = 1.0 / jnp.dot(base, col_scale, precision=lax.Precision.HIGHEST)

    def student_block(items):
        emb, plan, scale = items
        logits = contract_rows(emb, copies) / student_temp
        top = jnp.max(logits, axis=1, keepdims=True)
        expo = jnp.exp(logits - top)
        probs = expo / jnp.sum(expo, axis=1, keepdims=True)
        targets = scale[:, None] * plan * col_scale[None, :]
        return (probs - targets).astype(jnp.bfloat16)

    grad_logits = lax.map(student_block, (student_emb.reshape(count_blocks, block, width), base.reshape(count_blocks, block, -1), row_scale.reshape(count_blocks, block)))
    grad_logits = grad_logits.reshape(rows_total, -1)
    grad_student = jnp.dot(grad_logits, copies, preferred_element_type=jnp.float32) / student_temp
    grad_prototypes = lax.dot_general(grad_logits, student_emb, (((0,), (0,)), ((), ())), preferred_element_type=jnp.float32) / student_temp
    return grad_prototypes, grad_student
```

```python
import math

import jax
import jax.numpy as jnp
from jax import lax
from jax.sharding import PartitionSpec as P

ITERS = 3


teacher_temp = 0.07
student_temp = 0.1


def swap(x, axis, k):
    n = lax.axis_size(axis)
    return lax.ppermute(x, axis, [(i, i ^ (1 << k)) for i in range(n)])


def bits(axis):
    return int(math.log2(lax.axis_size(axis)))


def tree_butterfly(x, axis, combine):
    for k in range(bits(axis)):
        x = combine(x, swap(x, axis, k))
    return x


def sum_over(x, axis):
    return tree_butterfly(x, axis, lambda a, b: a + b)


def gather_blocks(x, axis):
    me = lax.axis_index(axis)
    for k in reversed(range(bits(axis))):
        bit = (me >> k) & 1
        other = swap(x, axis, k)
        buf = jnp.zeros((2,) + x.shape, x.dtype)
        buf = lax.dynamic_update_index_in_dim(buf, x, bit, 0)
        buf = lax.dynamic_update_index_in_dim(buf, other, 1 - bit, 0)
        x = buf.reshape((-1,) + x.shape[1:])
    return x


def scatter_blocks(x, axis):
    me = lax.axis_index(axis)
    for k in range(bits(axis)):
        bit = (me >> k) & 1
        x = x.reshape((2, x.shape[0] // 2) + x.shape[1:])
        keep = lax.dynamic_index_in_dim(x, bit, 0, keepdims=False)
        send = lax.dynamic_index_in_dim(x, 1 - bit, 0, keepdims=False)
        x = keep + swap(send, axis, k)
    return x


def contract_rows(left, right):
    return lax.dot_general(
        left, right, (((1,), (1,)), ((), ())), preferred_element_type=jnp.float32
    )


def combine_stats(first, second):
    teacher_top = jnp.maximum(first[0], second[0])
    student_top = jnp.maximum(first[1], second[1])
    total = first[2] * jnp.exp(first[1] - student_top) + second[2] * jnp.exp(
        second[1] - student_top
    )
    return jnp.stack([teacher_top, student_top, total])


def per_device(teacher_emb, student_emb, prototypes):
    copies = gather_blocks(prototypes.astype(jnp.bfloat16), "dp")
    rows_here = teacher_emb.shape[0]
    width = teacher_emb.shape[1]
    block = math.gcd(rows_here, 128)
    count_blocks = rows_here // block

    def teacher_block(emb):
        logits = contract_rows(emb, copies)
        top = jnp.max(logits, axis=1)
        return (jnp.exp((logits - top[:, None]) / teacher_temp), top)

    base_local, teacher_local = lax.map(
        teacher_block, teacher_emb.reshape(count_blocks, block, width)
    )
    base_local = base_local.reshape(rows_here, -1)
    teacher_local = teacher_local.reshape(rows_here)

    def student_stats(emb):
        logits = contract_rows(emb, copies) / student_temp
        top = jnp.max(logits, axis=1)
        return (top, jnp.sum(jnp.exp(logits - top[:, None]), axis=1))

    student_local, total_local = lax.map(
        student_stats, student_emb.reshape(count_blocks, block, width)
    )
    student_local = student_local.reshape(rows_here)
    total_local = total_local.reshape(rows_here)
    stats = tree_butterfly(
        jnp.stack([teacher_local, student_local, total_local]), "proto", combine_stats
    )
    teacher_top, student_top, total = stats[0], stats[1], stats[2]
    shift = jnp.exp((teacher_local - teacher_top) / teacher_temp)
    row_scale = jnp.ones((rows_here,), jnp.float32)
    col_scale = jnp.ones((base_local.shape[1],), jnp.float32)
    for step in range(ITERS):
        partial_cols = jnp.dot(row_scale * shift, base_local, precision=lax.Precision.HIGHEST)
        col_scale = 1.0 / sum_over(partial_cols, "dp")
        partial_rows = shift * jnp.dot(base_local, col_scale, precision=lax.Precision.HIGHEST)
        row_scale = 1.0 / sum_over(partial_rows, "proto")
    row_factor = row_scale * shift
    student_factor = jnp.exp(student_local - student_top) / total

    def gradient_block(items):
        emb, plan, factor, local_top, soft_factor = items
        logits = contract_rows(emb, copies) / student_temp
        probs = jnp.exp(logits - local_top[:, None]) * soft_factor[:, None]
        targets = factor[:, None] * plan * col_scale[None, :]
        grads = (probs - targets).astype(jnp.bfloat16)
        return (grads, jnp.dot(grads, copies, preferred_element_type=jnp.float32) / student_temp)

    grad_logits, student_terms = lax.map(
        gradient_block,
        (
            student_emb.reshape(count_blocks, block, width),
            base_local.reshape(count_blocks, block, -1),
            row_factor.reshape(count_blocks, block),
            student_local.reshape(count_blocks, block),
            student_factor.reshape(count_blocks, block),
        ),
    )
    grad_logits = grad_logits.reshape(rows_here, -1)
    grad_student = sum_over(student_terms.reshape(rows_here, width), "proto")
    grad_prototypes = scatter_blocks(
        lax.dot_general(
            grad_logits, student_emb, (((0,), (0,)), ((), ())), preferred_element_type=jnp.float32
        )
        / student_temp,
        "dp",
    )
    return (grad_prototypes, grad_student)


def solution(mesh):
    in_specs = (P("dp", None), P("dp", None), P(("dp", "proto"), None))
    out_specs = (P(("dp", "proto"), None), P("dp", None))
    return jax.shard_map(
        per_device, mesh=mesh, in_specs=in_specs, out_specs=out_specs, check_vma=False
    )
```

```python
import math

import jax
import jax.numpy as jnp
from jax import lax
from jax.sharding import PartitionSpec as P

ITERS = 3


teacher_temp = 0.07
student_temp = 0.1


def swap(x, axis, k):
    n = lax.axis_size(axis)
    return lax.ppermute(x, axis, [(i, i ^ (1 << k)) for i in range(n)])


def bits(axis):
    return int(math.log2(lax.axis_size(axis)))


GATHER_ORDER = ((6, 5, 4, 3, 2, 1, 0), (3, 2, 1, 6, 5, 4, 0))


def core_swap(x, axis, step, orders):
    n = lax.axis_size(axis)
    pairs = [(i, i ^ (1 << orders[i & 1][step])) for i in range(n)]
    return lax.ppermute(x, axis, pairs)


def core_bit(me, step, orders):
    k = jnp.where((me & 1) == 0, orders[0][step], orders[1][step])
    return (me >> k) & 1


def swap_halves(x):
    rows = x.shape[0]
    return x.reshape((8, 8, rows // 64) + x.shape[1:]).swapaxes(0, 1).reshape(x.shape)


def gather_blocks(x, axis):
    me = lax.axis_index(axis)
    steps = len(GATHER_ORDER[0])
    for step in range(steps):
        bit = core_bit(me, step, GATHER_ORDER)
        other = core_swap(x, axis, step, GATHER_ORDER)
        if step == steps - 1:
            other = swap_halves(other)
        buf = jnp.zeros((2,) + x.shape, x.dtype)
        buf = lax.dynamic_update_index_in_dim(buf, x, bit, 0)
        buf = lax.dynamic_update_index_in_dim(buf, other, 1 - bit, 0)
        x = buf.reshape((-1,) + x.shape[1:])
    return x


def scatter_blocks(x, axis):
    me = lax.axis_index(axis)
    orders = tuple(tuple(reversed(o)) for o in GATHER_ORDER)
    for step in range(len(orders[0])):
        bit = core_bit(me, step, orders)
        x = x.reshape((2, x.shape[0] // 2) + x.shape[1:])
        keep = lax.dynamic_index_in_dim(x, bit, 0, keepdims=False)
        send = lax.dynamic_index_in_dim(x, 1 - bit, 0, keepdims=False)
        other = core_swap(send, axis, step, orders)
        if step == 0:
            other = swap_halves(other)
        x = keep + other
    return x


def column_sum(x, axis):
    for k in range(bits(axis)):
        other = swap(x, axis, k)
        if k == 0:
            other = other.reshape(2, 8, 8, -1).swapaxes(1, 2).reshape(x.shape)
        x = x + other
    return x


def proto_sum(x):
    parts = lax.all_gather(x, "proto", axis=0, tiled=False)
    total = parts[0]
    for j in range(1, parts.shape[0]):
        total = total + parts[j]
    return total


def contract_rows(left, right):
    return lax.dot_general(
        left, right, (((1,), (1,)), ((), ())), preferred_element_type=jnp.float32
    )


def combine_stats(first, second):
    teacher_top = jnp.maximum(first[0], second[0])
    student_top = jnp.maximum(first[1], second[1])
    total = first[2] * jnp.exp(first[1] - student_top) + second[2] * jnp.exp(
        second[1] - student_top
    )
    return jnp.stack([teacher_top, student_top, total])


def per_device(teacher_emb, student_emb, prototypes):
    copies = gather_blocks(prototypes.astype(jnp.bfloat16), "dp")
    rows_here = teacher_emb.shape[0]
    width = teacher_emb.shape[1]
    block = math.gcd(rows_here, 128)
    count_blocks = rows_here // block

    def teacher_block(emb):
        logits = contract_rows(emb, copies)
        top = jnp.max(logits, axis=1)
        return (jnp.exp((logits - top[:, None]) / teacher_temp), top)

    base_local, teacher_local = lax.map(
        teacher_block, teacher_emb.reshape(count_blocks, block, width)
    )
    base_local = base_local.reshape(rows_here, -1)
    teacher_local = teacher_local.reshape(rows_here)

    def student_stats(emb):
        logits = contract_rows(emb, copies) / student_temp
        top = jnp.max(logits, axis=1)
        return (top, jnp.sum(jnp.exp(logits - top[:, None]), axis=1))

    student_local, total_local = lax.map(
        student_stats, student_emb.reshape(count_blocks, block, width)
    )
    student_local = student_local.reshape(rows_here)
    total_local = total_local.reshape(rows_here)
    every = lax.all_gather(
        jnp.stack([teacher_local, student_local, total_local]), "proto", axis=0, tiled=False
    )
    stats = every[0]
    for j in range(1, every.shape[0]):
        stats = combine_stats(stats, every[j])
    teacher_top, student_top, total = stats[0], stats[1], stats[2]
    shift = jnp.exp((teacher_local - teacher_top) / teacher_temp)
    row_scale = jnp.ones((rows_here,), jnp.float32)
    col_scale = jnp.ones((base_local.shape[1],), jnp.float32)
    for step in range(ITERS):
        partial_cols = jnp.dot(row_scale * shift, base_local, precision=lax.Precision.HIGHEST)
        col_scale = 1.0 / column_sum(partial_cols, "dp")
        partial_rows = shift * jnp.dot(base_local, col_scale, precision=lax.Precision.HIGHEST)
        row_scale = 1.0 / lax.psum(partial_rows, "proto")
    row_factor = row_scale * shift
    student_factor = jnp.exp(student_local - student_top) / total

    def gradient_block(items):
        emb, plan, factor, local_top, soft_factor = items
        logits = contract_rows(emb, copies) / student_temp
        probs = jnp.exp(logits - local_top[:, None]) * soft_factor[:, None]
        targets = factor[:, None] * plan * col_scale[None, :]
        grads = (probs - targets).astype(jnp.bfloat16)
        return (grads, jnp.dot(grads, copies, preferred_element_type=jnp.float32) / student_temp)

    grad_logits, student_terms = lax.map(
        gradient_block,
        (
            student_emb.reshape(count_blocks, block, width),
            base_local.reshape(count_blocks, block, -1),
            row_factor.reshape(count_blocks, block),
            student_local.reshape(count_blocks, block),
            student_factor.reshape(count_blocks, block),
        ),
    )
    grad_logits = grad_logits.reshape(rows_here, -1)
    grad_student = proto_sum(student_terms.reshape(rows_here, width))
    grad_prototypes = scatter_blocks(
        lax.dot_general(
            grad_logits, student_emb, (((0,), (0,)), ((), ())), preferred_element_type=jnp.float32
        )
        / student_temp,
        "dp",
    )
    return (grad_prototypes, grad_student)


def solution(mesh):
    in_specs = (P("dp", None), P("dp", None), P(("dp", "proto"), None))
    out_specs = (P(("dp", "proto"), None), P("dp", None))
    return jax.shard_map(
        per_device, mesh=mesh, in_specs=in_specs, out_specs=out_specs, check_vma=False
    )
```

```python
import math

import jax
import jax.numpy as jnp
from jax import lax
from jax.sharding import PartitionSpec as P

ITERS = 3


teacher_temp = 0.07
student_temp = 0.1


def swap(x, axis, k):
    n = lax.axis_size(axis)
    return lax.ppermute(x, axis, [(i, i ^ (1 << k)) for i in range(n)])


def bits(axis):
    return int(math.log2(lax.axis_size(axis)))


GATHER_ORDER = ((6, 5, 4, 3, 2, 1, 0), (3, 2, 1, 6, 5, 4, 0))


def core_swap(x, axis, step, orders):
    n = lax.axis_size(axis)
    pairs = [(i, i ^ (1 << orders[i & 1][step])) for i in range(n)]
    return lax.ppermute(x, axis, pairs)


def core_bit(me, step, orders):
    k = jnp.where((me & 1) == 0, orders[0][step], orders[1][step])
    return (me >> k) & 1


def swap_halves(x):
    rows = x.shape[0]
    return x.reshape((8, 8, rows // 64) + x.shape[1:]).swapaxes(0, 1).reshape(x.shape)


def gather_blocks(x, axis):
    me = lax.axis_index(axis)
    steps = len(GATHER_ORDER[0])
    for step in range(steps):
        bit = core_bit(me, step, GATHER_ORDER)
        other = core_swap(x, axis, step, GATHER_ORDER)
        if step == steps - 1:
            other = swap_halves(other)
        buf = jnp.zeros((2,) + x.shape, x.dtype)
        buf = lax.dynamic_update_index_in_dim(buf, x, bit, 0)
        buf = lax.dynamic_update_index_in_dim(buf, other, 1 - bit, 0)
        x = buf.reshape((-1,) + x.shape[1:])
    return x


def scatter_blocks(x, axis):
    me = lax.axis_index(axis)
    orders = tuple(tuple(reversed(o)) for o in GATHER_ORDER)
    for step in range(len(orders[0])):
        bit = core_bit(me, step, orders)
        x = x.reshape((2, x.shape[0] // 2) + x.shape[1:])
        keep = lax.dynamic_index_in_dim(x, bit, 0, keepdims=False)
        send = lax.dynamic_index_in_dim(x, 1 - bit, 0, keepdims=False)
        other = core_swap(send, axis, step, orders)
        if step == 0:
            other = swap_halves(other)
        x = keep + other
    return x


def sum_over(x, axis):
    for k in range(bits(axis)):
        x = x + swap(x, axis, k)
    return x


def column_sum(x, axis):
    for k in range(bits(axis)):
        other = swap(x, axis, k)
        if k == 0:
            other = other.reshape(2, 8, 8, -1).swapaxes(1, 2).reshape(x.shape)
        x = x + other
    return x


def contract_rows(left, right):
    return lax.dot_general(
        left, right, (((1,), (1,)), ((), ())), preferred_element_type=jnp.float32
    )


def combine_stats(first, second):
    teacher_top = jnp.maximum(first[0], second[0])
    student_top = jnp.maximum(first[1], second[1])
    total = first[2] * jnp.exp(first[1] - student_top) + second[2] * jnp.exp(
        second[1] - student_top
    )
    return jnp.stack([teacher_top, student_top, total])


def per_device(teacher_emb, student_emb, prototypes):
    copies = gather_blocks(prototypes.astype(jnp.bfloat16), "dp")
    rows_here = teacher_emb.shape[0]
    width = teacher_emb.shape[1]
    block = math.gcd(rows_here, 128)
    count_blocks = rows_here // block

    def teacher_block(emb):
        logits = contract_rows(emb, copies)
        top = jnp.max(logits, axis=1)
        return (jnp.exp((logits - top[:, None]) / teacher_temp), top)

    base_local, teacher_local = lax.map(
        teacher_block, teacher_emb.reshape(count_blocks, block, width)
    )
    base_local = base_local.reshape(rows_here, -1)
    teacher_local = teacher_local.reshape(rows_here)

    def student_stats(emb):
        logits = contract_rows(emb, copies) / student_temp
        top = jnp.max(logits, axis=1)
        return (top, jnp.sum(jnp.exp(logits - top[:, None]), axis=1))

    student_local, total_local = lax.map(
        student_stats, student_emb.reshape(count_blocks, block, width)
    )
    student_local = student_local.reshape(rows_here)
    total_local = total_local.reshape(rows_here)
    every = lax.all_gather(
        jnp.stack([teacher_local, student_local, total_local]), "proto", axis=0, tiled=False
    )
    stats = every[0]
    for j in range(1, every.shape[0]):
        stats = combine_stats(stats, every[j])
    teacher_top, student_top, total = stats[0], stats[1], stats[2]
    shift = jnp.exp((teacher_local - teacher_top) / teacher_temp)
    row_scale = jnp.ones((rows_here,), jnp.float32)
    col_scale = jnp.ones((base_local.shape[1],), jnp.float32)
    for step in range(ITERS):
        partial_cols = jnp.dot(row_scale * shift, base_local, precision=lax.Precision.HIGHEST)
        col_scale = 1.0 / column_sum(partial_cols, "dp")
        partial_rows = shift * jnp.dot(base_local, col_scale, precision=lax.Precision.HIGHEST)
        row_scale = 1.0 / sum_over(partial_rows, "proto")
    row_factor = row_scale * shift
    student_factor = jnp.exp(student_local - student_top) / total

    def gradient_block(items):
        emb, plan, factor, local_top, soft_factor = items
        logits = contract_rows(emb, copies) / student_temp
        probs = jnp.exp(logits - local_top[:, None]) * soft_factor[:, None]
        targets = factor[:, None] * plan * col_scale[None, :]
        grads = (probs - targets).astype(jnp.bfloat16)
        return (grads, jnp.dot(grads, copies, preferred_element_type=jnp.float32) / student_temp)

    grad_logits, student_terms = lax.map(
        gradient_block,
        (
            student_emb.reshape(count_blocks, block, width),
            base_local.reshape(count_blocks, block, -1),
            row_factor.reshape(count_blocks, block),
            student_local.reshape(count_blocks, block),
            student_factor.reshape(count_blocks, block),
        ),
    )
    grad_logits = grad_logits.reshape(rows_here, -1)
    grad_student = sum_over(student_terms.reshape(rows_here, width), "proto")
    grad_prototypes = scatter_blocks(
        lax.dot_general(
            grad_logits, student_emb, (((0,), (0,)), ((), ())), preferred_element_type=jnp.float32
        )
        / student_temp,
        "dp",
    )
    return (grad_prototypes, grad_student)


def solution(mesh):
    in_specs = (P("dp", None), P("dp", None), P(("dp", "proto"), None))
    out_specs = (P(("dp", "proto"), None), P("dp", None))
    return jax.shard_map(
        per_device, mesh=mesh, in_specs=in_specs, out_specs=out_specs, check_vma=False
    )
```

```python
import math

import jax
import jax.numpy as jnp
from jax import lax
from jax.sharding import PartitionSpec as P

ITERS = 3


teacher_temp = 0.07
student_temp = 0.1


def swap(x, axis, k):
    n = lax.axis_size(axis)
    return lax.ppermute(x, axis, [(i, i ^ (1 << k)) for i in range(n)])


def bits(axis):
    return int(math.log2(lax.axis_size(axis)))


GATHER_ORDER = ((6, 5, 4, 3, 2, 1, 0), (3, 2, 1, 6, 5, 4, 0))


def core_swap(x, axis, step, orders):
    n = lax.axis_size(axis)
    pairs = [(i, i ^ (1 << orders[i & 1][step])) for i in range(n)]
    return lax.ppermute(x, axis, pairs)


def core_bit(me, step, orders):
    k = jnp.where((me & 1) == 0, orders[0][step], orders[1][step])
    return (me >> k) & 1


def swap_halves(x):
    rows = x.shape[0]
    return x.reshape((8, 8, rows // 64) + x.shape[1:]).swapaxes(0, 1).reshape(x.shape)


def gather_blocks(x, axis):
    me = lax.axis_index(axis)
    steps = len(GATHER_ORDER[0])
    for step in range(steps):
        bit = core_bit(me, step, GATHER_ORDER)
        other = core_swap(x, axis, step, GATHER_ORDER)
        if step == steps - 1:
            other = swap_halves(other)
        buf = jnp.zeros((2,) + x.shape, x.dtype)
        buf = lax.dynamic_update_index_in_dim(buf, x, bit, 0)
        buf = lax.dynamic_update_index_in_dim(buf, other, 1 - bit, 0)
        x = buf.reshape((-1,) + x.shape[1:])
    return x


def scatter_blocks(x, axis):
    me = lax.axis_index(axis)
    orders = tuple(tuple(reversed(o)) for o in GATHER_ORDER)
    for step in range(len(orders[0])):
        bit = core_bit(me, step, orders)
        x = x.reshape((2, x.shape[0] // 2) + x.shape[1:])
        keep = lax.dynamic_index_in_dim(x, bit, 0, keepdims=False)
        send = lax.dynamic_index_in_dim(x, 1 - bit, 0, keepdims=False)
        other = core_swap(send, axis, step, orders)
        if step == 0:
            other = swap_halves(other)
        x = keep + other
    return x


def sum_over(x, axis):
    for k in range(bits(axis)):
        x = x + swap(x, axis, k)
    return x


def column_sum(x, axis):
    for k in range(bits(axis)):
        other = swap(x, axis, k)
        if k == 0:
            other = other.reshape(2, 8, 8, -1).swapaxes(1, 2).reshape(x.shape)
        x = x + other
    return x


def contract_rows(left, right):
    return lax.dot_general(
        left, right, (((1,), (1,)), ((), ())), preferred_element_type=jnp.float32
    )


def combine_stats(first, second):
    teacher_top = jnp.maximum(first[0], second[0])
    student_top = jnp.maximum(first[1], second[1])
    total = first[2] * jnp.exp(first[1] - student_top) + second[2] * jnp.exp(
        second[1] - student_top
    )
    return jnp.stack([teacher_top, student_top, total])


def per_device(teacher_emb, student_emb, prototypes):
    copies = gather_blocks(prototypes.astype(jnp.bfloat16), "dp")
    rows_here = teacher_emb.shape[0]
    width = teacher_emb.shape[1]
    block = math.gcd(rows_here, 128)
    count_blocks = rows_here // block

    def teacher_block(emb):
        logits = contract_rows(emb, copies)
        top = jnp.max(logits, axis=1)
        return (jnp.exp((logits - top[:, None]) / teacher_temp), top)

    base_local, teacher_local = lax.map(
        teacher_block, teacher_emb.reshape(count_blocks, block, width)
    )
    base_local = base_local.reshape(rows_here, -1)
    teacher_local = teacher_local.reshape(rows_here)

    def student_stats(emb):
        logits = contract_rows(emb, copies) / student_temp
        top = jnp.max(logits, axis=1)
        return (top, jnp.sum(jnp.exp(logits - top[:, None]), axis=1))

    student_local, total_local = lax.map(
        student_stats, student_emb.reshape(count_blocks, block, width)
    )
    student_local = student_local.reshape(rows_here)
    total_local = total_local.reshape(rows_here)
    every = lax.all_gather(
        jnp.stack([teacher_local, student_local, total_local]), "proto", axis=0, tiled=False
    )
    stats = every[0]
    for j in range(1, every.shape[0]):
        stats = combine_stats(stats, every[j])
    teacher_top, student_top, total = stats[0], stats[1], stats[2]
    shift = jnp.exp((teacher_local - teacher_top) / teacher_temp)
    row_scale = jnp.ones((rows_here,), jnp.float32)
    col_scale = jnp.ones((base_local.shape[1],), jnp.float32)
    for step in range(ITERS):
        partial_cols = jnp.sum((row_scale * shift)[:, None] * base_local, axis=0)
        col_scale = 1.0 / column_sum(partial_cols, "dp")
        partial_rows = shift * jnp.sum(base_local * col_scale[None, :], axis=1)
        row_scale = 1.0 / sum_over(partial_rows, "proto")
    row_factor = row_scale * shift
    student_factor = jnp.exp(student_local - student_top) / total

    def gradient_block(items):
        emb, plan, factor, local_top, soft_factor = items
        logits = contract_rows(emb, copies) / student_temp
        probs = jnp.exp(logits - local_top[:, None]) * soft_factor[:, None]
        targets = factor[:, None] * plan * col_scale[None, :]
        grads = (probs - targets).astype(jnp.bfloat16)
        return (grads, jnp.dot(grads, copies, preferred_element_type=jnp.float32) / student_temp)

    grad_logits, student_terms = lax.map(
        gradient_block,
        (
            student_emb.reshape(count_blocks, block, width),
            base_local.reshape(count_blocks, block, -1),
            row_factor.reshape(count_blocks, block),
            student_local.reshape(count_blocks, block),
            student_factor.reshape(count_blocks, block),
        ),
    )
    grad_logits = grad_logits.reshape(rows_here, -1)
    grad_student = sum_over(student_terms.reshape(rows_here, width), "proto")
    grad_prototypes = scatter_blocks(
        lax.dot_general(
            grad_logits, student_emb, (((0,), (0,)), ((), ())), preferred_element_type=jnp.float32
        )
        / student_temp,
        "dp",
    )
    return (grad_prototypes, grad_student)


def solution(mesh):
    in_specs = (P("dp", None), P("dp", None), P(("dp", "proto"), None))
    out_specs = (P(("dp", "proto"), None), P("dp", None))
    return jax.shard_map(
        per_device, mesh=mesh, in_specs=in_specs, out_specs=out_specs, check_vma=False
    )
```

```python
import math

import jax
import jax.numpy as jnp
from jax import lax
from jax.sharding import PartitionSpec as P

ITERS = 3


teacher_temp = 0.07
student_temp = 0.1


def swap(x, axis, k):
    n = lax.axis_size(axis)
    return lax.ppermute(x, axis, [(i, i ^ (1 << k)) for i in range(n)])


def bits(axis):
    return int(math.log2(lax.axis_size(axis)))


GATHER_ORDER = ((6, 5, 4, 3, 2, 1, 0), (3, 2, 1, 6, 5, 4, 0))


def core_swap(x, axis, step, orders):
    n = lax.axis_size(axis)
    pairs = [(i, i ^ (1 << orders[i & 1][step])) for i in range(n)]
    return lax.ppermute(x, axis, pairs)


def core_bit(me, step, orders):
    k = jnp.where((me & 1) == 0, orders[0][step], orders[1][step])
    return (me >> k) & 1


def swap_halves(x):
    rows = x.shape[0]
    return x.reshape((8, 8, rows // 64) + x.shape[1:]).swapaxes(0, 1).reshape(x.shape)


def gather_blocks(x, axis):
    me = lax.axis_index(axis)
    steps = len(GATHER_ORDER[0])
    for step in range(steps):
        bit = core_bit(me, step, GATHER_ORDER)
        other = core_swap(x, axis, step, GATHER_ORDER)
        if step == steps - 1:
            other = swap_halves(other)
        buf = jnp.zeros((2,) + x.shape, x.dtype)
        buf = lax.dynamic_update_index_in_dim(buf, x, bit, 0)
        buf = lax.dynamic_update_index_in_dim(buf, other, 1 - bit, 0)
        x = buf.reshape((-1,) + x.shape[1:])
    return x


def scatter_blocks(x, axis):
    me = lax.axis_index(axis)
    orders = tuple(tuple(reversed(o)) for o in GATHER_ORDER)
    for step in range(len(orders[0])):
        bit = core_bit(me, step, orders)
        x = x.reshape((2, x.shape[0] // 2) + x.shape[1:])
        keep = lax.dynamic_index_in_dim(x, bit, 0, keepdims=False)
        send = lax.dynamic_index_in_dim(x, 1 - bit, 0, keepdims=False)
        other = core_swap(send, axis, step, orders)
        if step == 0:
            other = swap_halves(other)
        x = keep + other
    return x


def sum_over(x, axis):
    for k in range(bits(axis)):
        x = x + swap(x, axis, k)
    return x


def column_sum(x, axis):
    for k in range(bits(axis)):
        other = swap(x, axis, k)
        if k == 0:
            other = other.reshape(2, 8, 8, -1).swapaxes(1, 2).reshape(x.shape)
        x = x + other
    return x


def contract_rows(left, right):
    return lax.dot_general(
        left, right, (((1,), (1,)), ((), ())), preferred_element_type=jnp.float32
    )


def combine_stats(first, second):
    teacher_top = jnp.maximum(first[0], second[0])
    student_top = jnp.maximum(first[1], second[1])
    total = first[2] * jnp.exp(first[1] - student_top) + second[2] * jnp.exp(
        second[1] - student_top
    )
    return jnp.stack([teacher_top, student_top, total])


def per_device(teacher_emb, student_emb, prototypes):
    copies = gather_blocks(prototypes.astype(jnp.bfloat16), "dp")
    rows_here = teacher_emb.shape[0]
    width = teacher_emb.shape[1]
    block = math.gcd(rows_here, 128)
    count_blocks = rows_here // block

    def teacher_block(emb):
        logits = contract_rows(emb, copies)
        top = jnp.max(logits, axis=1)
        return (jnp.exp((logits - top[:, None]) / teacher_temp), top)

    base_local, teacher_local = lax.map(
        teacher_block, teacher_emb.reshape(count_blocks, block, width)
    )
    base_local = base_local.reshape(rows_here, -1)
    teacher_local = teacher_local.reshape(rows_here)

    def student_stats(emb):
        logits = contract_rows(emb, copies) / student_temp
        top = jnp.max(logits, axis=1)
        return (top, jnp.sum(jnp.exp(logits - top[:, None]), axis=1))

    student_local, total_local = lax.map(
        student_stats, student_emb.reshape(count_blocks, block, width)
    )
    student_local = student_local.reshape(rows_here)
    total_local = total_local.reshape(rows_here)
    every = lax.all_gather(
        jnp.stack([teacher_local, student_local, total_local]), "proto", axis=0, tiled=False
    )
    stats = every[0]
    for j in range(1, every.shape[0]):
        stats = combine_stats(stats, every[j])
    teacher_top, student_top, total = stats[0], stats[1], stats[2]
    shift = jnp.exp((teacher_local - teacher_top) / teacher_temp)
    row_scale = jnp.ones((rows_here,), jnp.float32)
    col_scale = jnp.ones((base_local.shape[1],), jnp.float32)
    for step in range(ITERS):
        partial_cols = jnp.sum((row_scale * shift)[:, None] * base_local, axis=0)
        col_scale = 1.0 / column_sum(partial_cols, "dp")
        partial_rows = shift * jnp.sum(base_local * col_scale[None, :], axis=1)
        row_scale = 1.0 / lax.psum(partial_rows, "proto")
    row_factor = row_scale * shift
    student_factor = jnp.exp(student_local - student_top) / total

    def gradient_block(items):
        emb, plan, factor, local_top, soft_factor = items
        logits = contract_rows(emb, copies) / student_temp
        probs = jnp.exp(logits - local_top[:, None]) * soft_factor[:, None]
        targets = factor[:, None] * plan * col_scale[None, :]
        grads = (probs - targets).astype(jnp.bfloat16)
        return (grads, jnp.dot(grads, copies, preferred_element_type=jnp.float32) / student_temp)

    grad_logits, student_terms = lax.map(
        gradient_block,
        (
            student_emb.reshape(count_blocks, block, width),
            base_local.reshape(count_blocks, block, -1),
            row_factor.reshape(count_blocks, block),
            student_local.reshape(count_blocks, block),
            student_factor.reshape(count_blocks, block),
        ),
    )
    grad_logits = grad_logits.reshape(rows_here, -1)
    grad_student = sum_over(student_terms.reshape(rows_here, width), "proto")
    grad_prototypes = scatter_blocks(
        lax.dot_general(
            grad_logits, student_emb, (((0,), (0,)), ((), ())), preferred_element_type=jnp.float32
        )
        / student_temp,
        "dp",
    )
    return (grad_prototypes, grad_student)


def solution(mesh):
    in_specs = (P("dp", None), P("dp", None), P(("dp", "proto"), None))
    out_specs = (P(("dp", "proto"), None), P("dp", None))
    return jax.shard_map(
        per_device, mesh=mesh, in_specs=in_specs, out_specs=out_specs, check_vma=False
    )
```

```python
import math

import jax
import jax.numpy as jnp
from jax import lax
from jax.sharding import PartitionSpec as P

ITERS = 3


teacher_temp = 0.07
student_temp = 0.1


def swap(x, axis, k):
    n = lax.axis_size(axis)
    return lax.ppermute(x, axis, [(i, i ^ (1 << k)) for i in range(n)])


def bits(axis):
    return int(math.log2(lax.axis_size(axis)))


GATHER_ORDER = ((6, 3, 5, 2, 4, 1, 0), (3, 6, 2, 5, 1, 4, 0))


def core_swap(x, axis, step, orders):
    n = lax.axis_size(axis)
    pairs = [(i, i ^ (1 << orders[i & 1][step])) for i in range(n)]
    return lax.ppermute(x, axis, pairs)


def core_bit(me, step, orders):
    k = jnp.where((me & 1) == 0, orders[0][step], orders[1][step])
    return (me >> k) & 1


def swap_halves(x):
    shape = (2,) * 6 + (x.shape[0] // 64,) + x.shape[1:]
    dims = (1, 0, 3, 2, 5, 4) + tuple(range(6, len(shape)))
    return x.reshape(shape).transpose(dims).reshape(x.shape)


def gather_blocks(x, axis):
    me = lax.axis_index(axis)
    steps = len(GATHER_ORDER[0])
    for step in range(steps):
        bit = core_bit(me, step, GATHER_ORDER)
        other = core_swap(x, axis, step, GATHER_ORDER)
        if step == steps - 1:
            other = swap_halves(other)
        buf = jnp.zeros((2,) + x.shape, x.dtype)
        buf = lax.dynamic_update_index_in_dim(buf, x, bit, 0)
        buf = lax.dynamic_update_index_in_dim(buf, other, 1 - bit, 0)
        x = buf.reshape((-1,) + x.shape[1:])
    return x


def scatter_blocks(x, axis):
    me = lax.axis_index(axis)
    orders = tuple(tuple(reversed(o)) for o in GATHER_ORDER)
    for step in range(len(orders[0])):
        bit = core_bit(me, step, orders)
        x = x.reshape((2, x.shape[0] // 2) + x.shape[1:])
        keep = lax.dynamic_index_in_dim(x, bit, 0, keepdims=False)
        send = lax.dynamic_index_in_dim(x, 1 - bit, 0, keepdims=False)
        other = core_swap(send, axis, step, orders)
        if step == 0:
            other = swap_halves(other)
        x = keep + other
    return x


def sum_over(x, axis):
    for k in range(bits(axis)):
        x = x + swap(x, axis, k)
    return x


def column_sum(x, axis):
    for k in range(bits(axis)):
        other = swap(x, axis, k)
        if k == 0:
            other = jax.vmap(swap_halves)(other.reshape(2, -1, 1)).reshape(x.shape)
        x = x + other
    return x


def contract_rows(left, right):
    return lax.dot_general(
        left, right, (((1,), (1,)), ((), ())), preferred_element_type=jnp.float32
    )


def combine_stats(first, second):
    teacher_top = jnp.maximum(first[0], second[0])
    student_top = jnp.maximum(first[1], second[1])
    total = first[2] * jnp.exp(first[1] - student_top) + second[2] * jnp.exp(
        second[1] - student_top
    )
    return jnp.stack([teacher_top, student_top, total])


def per_device(teacher_emb, student_emb, prototypes):
    copies = gather_blocks(prototypes.astype(jnp.bfloat16), "dp")
    rows_here = teacher_emb.shape[0]
    width = teacher_emb.shape[1]
    block = math.gcd(rows_here, 128)
    count_blocks = rows_here // block

    def teacher_block(emb):
        logits = contract_rows(emb, copies)
        top = jnp.max(logits, axis=1)
        return (jnp.exp((logits - top[:, None]) / teacher_temp), top)

    base_local, teacher_local = lax.map(
        teacher_block, teacher_emb.reshape(count_blocks, block, width)
    )
    base_local = base_local.reshape(rows_here, -1)
    teacher_local = teacher_local.reshape(rows_here)

    def student_stats(emb):
        logits = contract_rows(emb, copies) / student_temp
        top = jnp.max(logits, axis=1)
        return (top, jnp.sum(jnp.exp(logits - top[:, None]), axis=1))

    student_local, total_local = lax.map(
        student_stats, student_emb.reshape(count_blocks, block, width)
    )
    student_local = student_local.reshape(rows_here)
    total_local = total_local.reshape(rows_here)
    every = lax.all_gather(
        jnp.stack([teacher_local, student_local, total_local]), "proto", axis=0, tiled=False
    )
    stats = every[0]
    for j in range(1, every.shape[0]):
        stats = combine_stats(stats, every[j])
    teacher_top, student_top, total = stats[0], stats[1], stats[2]
    shift = jnp.exp((teacher_local - teacher_top) / teacher_temp)
    row_scale = jnp.ones((rows_here,), jnp.float32)
    col_scale = jnp.ones((base_local.shape[1],), jnp.float32)
    for step in range(ITERS):
        partial_cols = jnp.sum((row_scale * shift)[:, None] * base_local, axis=0)
        col_scale = 1.0 / column_sum(partial_cols, "dp")
        partial_rows = shift * jnp.sum(base_local * col_scale[None, :], axis=1)
        row_scale = 1.0 / lax.psum(partial_rows, "proto")
    row_factor = row_scale * shift
    student_factor = jnp.exp(student_local - student_top) / total

    def gradient_block(items):
        emb, plan, factor, local_top, soft_factor = items
        logits = contract_rows(emb, copies) / student_temp
        probs = jnp.exp(logits - local_top[:, None]) * soft_factor[:, None]
        targets = factor[:, None] * plan * col_scale[None, :]
        grads = (probs - targets).astype(jnp.bfloat16)
        return (grads, jnp.dot(grads, copies, preferred_element_type=jnp.float32) / student_temp)

    grad_logits, student_terms = lax.map(
        gradient_block,
        (
            student_emb.reshape(count_blocks, block, width),
            base_local.reshape(count_blocks, block, -1),
            row_factor.reshape(count_blocks, block),
            student_local.reshape(count_blocks, block),
            student_factor.reshape(count_blocks, block),
        ),
    )
    grad_logits = grad_logits.reshape(rows_here, -1)
    grad_student = sum_over(student_terms.reshape(rows_here, width), "proto")
    grad_prototypes = scatter_blocks(
        lax.dot_general(
            grad_logits, student_emb, (((0,), (0,)), ((), ())), preferred_element_type=jnp.float32
        )
        / student_temp,
        "dp",
    )
    return (grad_prototypes, grad_student)


def solution(mesh):
    in_specs = (P("dp", None), P("dp", None), P(("dp", "proto"), None))
    out_specs = (P(("dp", "proto"), None), P("dp", None))
    return jax.shard_map(
        per_device, mesh=mesh, in_specs=in_specs, out_specs=out_specs, check_vma=False
    )
```

```python
import math

import jax
import jax.numpy as jnp
from jax import lax
from jax.sharding import PartitionSpec as P

ITERS = 3


teacher_temp = 0.07
student_temp = 0.1


def swap(x, axis, k):
    n = lax.axis_size(axis)
    return lax.ppermute(x, axis, [(i, i ^ (1 << k)) for i in range(n)])


def bits(axis):
    return int(math.log2(lax.axis_size(axis)))


GATHER_ORDER = ((6, 3, 5, 2, 4, 1, 0), (3, 6, 2, 5, 1, 4, 0))


def core_swap(x, axis, step, orders):
    n = lax.axis_size(axis)
    pairs = [(i, i ^ (1 << orders[i & 1][step])) for i in range(n)]
    return lax.ppermute(x, axis, pairs)


def core_bit(me, step, orders):
    k = jnp.where((me & 1) == 0, orders[0][step], orders[1][step])
    return (me >> k) & 1


def swap_halves(x):
    shape = (2,) * 6 + (x.shape[0] // 64,) + x.shape[1:]
    dims = (1, 0, 3, 2, 5, 4) + tuple(range(6, len(shape)))
    return x.reshape(shape).transpose(dims).reshape(x.shape)


def gather_blocks(x, axis):
    me = lax.axis_index(axis)
    steps = len(GATHER_ORDER[0])
    for step in range(steps):
        bit = core_bit(me, step, GATHER_ORDER)
        other = core_swap(x, axis, step, GATHER_ORDER)
        if step == steps - 1:
            other = swap_halves(other)
        buf = jnp.zeros((2,) + x.shape, x.dtype)
        buf = lax.dynamic_update_index_in_dim(buf, x, bit, 0)
        buf = lax.dynamic_update_index_in_dim(buf, other, 1 - bit, 0)
        x = buf.reshape((-1,) + x.shape[1:])
    return x


def scatter_blocks(x, axis):
    me = lax.axis_index(axis)
    orders = tuple(tuple(reversed(o)) for o in GATHER_ORDER)
    for step in range(len(orders[0])):
        bit = core_bit(me, step, orders)
        x = x.reshape((2, x.shape[0] // 2) + x.shape[1:])
        keep = lax.dynamic_index_in_dim(x, bit, 0, keepdims=False)
        send = lax.dynamic_index_in_dim(x, 1 - bit, 0, keepdims=False)
        other = core_swap(send, axis, step, orders)
        if step == 0:
            other = swap_halves(other)
        x = keep + other
    return x


def sum_over(x, axis):
    for k in range(bits(axis)):
        x = x + swap(x, axis, k)
    return x


def column_sum(x, axis):
    for k in range(bits(axis)):
        other = swap(x, axis, k)
        if k == 0:
            other = jax.vmap(swap_halves)(other.reshape(2, -1, 1)).reshape(x.shape)
        x = x + other
    return x


def contract_rows(left, right):
    return lax.dot_general(
        left, right, (((1,), (1,)), ((), ())), preferred_element_type=jnp.float32
    )


def combine_stats(first, second):
    teacher_top = jnp.maximum(first[0], second[0])
    student_top = jnp.maximum(first[1], second[1])
    total = first[2] * jnp.exp(first[1] - student_top) + second[2] * jnp.exp(
        second[1] - student_top
    )
    return jnp.stack([teacher_top, student_top, total])


def per_device(teacher_emb, student_emb, prototypes):
    copies = gather_blocks(prototypes.astype(jnp.bfloat16), "dp")
    rows_here = teacher_emb.shape[0]
    width = teacher_emb.shape[1]
    block = rows_here
    count_blocks = rows_here // block

    def teacher_block(emb):
        logits = contract_rows(emb, copies)
        top = jnp.max(logits, axis=1)
        return (jnp.exp((logits - top[:, None]) / teacher_temp), top)

    base_local, teacher_local = lax.map(
        teacher_block, teacher_emb.reshape(count_blocks, block, width)
    )
    base_local = base_local.reshape(rows_here, -1)
    teacher_local = teacher_local.reshape(rows_here)

    def student_stats(emb):
        logits = contract_rows(emb, copies) / student_temp
        top = jnp.max(logits, axis=1)
        return (top, jnp.sum(jnp.exp(logits - top[:, None]), axis=1))

    student_local, total_local = lax.map(
        student_stats, student_emb.reshape(count_blocks, block, width)
    )
    student_local = student_local.reshape(rows_here)
    total_local = total_local.reshape(rows_here)
    every = lax.all_gather(
        jnp.stack([teacher_local, student_local, total_local]), "proto", axis=0, tiled=False
    )
    stats = every[0]
    for j in range(1, every.shape[0]):
        stats = combine_stats(stats, every[j])
    teacher_top, student_top, total = stats[0], stats[1], stats[2]
    shift = jnp.exp((teacher_local - teacher_top) / teacher_temp)
    row_scale = jnp.ones((rows_here,), jnp.float32)
    col_scale = jnp.ones((base_local.shape[1],), jnp.float32)
    for step in range(ITERS):
        partial_cols = jnp.sum((row_scale * shift)[:, None] * base_local, axis=0)
        col_scale = 1.0 / column_sum(partial_cols, "dp")
        partial_rows = shift * jnp.sum(base_local * col_scale[None, :], axis=1)
        row_scale = 1.0 / lax.psum(partial_rows, "proto")
    row_factor = row_scale * shift
    student_factor = jnp.exp(student_local - student_top) / total

    def gradient_block(items):
        emb, plan, factor, local_top, soft_factor = items
        logits = contract_rows(emb, copies) / student_temp
        probs = jnp.exp(logits - local_top[:, None]) * soft_factor[:, None]
        targets = factor[:, None] * plan * col_scale[None, :]
        grads = (probs - targets).astype(jnp.bfloat16)
        return (grads, jnp.dot(grads, copies, preferred_element_type=jnp.float32) / student_temp)

    grad_logits, student_terms = lax.map(
        gradient_block,
        (
            student_emb.reshape(count_blocks, block, width),
            base_local.reshape(count_blocks, block, -1),
            row_factor.reshape(count_blocks, block),
            student_local.reshape(count_blocks, block),
            student_factor.reshape(count_blocks, block),
        ),
    )
    grad_logits = grad_logits.reshape(rows_here, -1)
    grad_student = sum_over(student_terms.reshape(rows_here, width), "proto")
    grad_prototypes = scatter_blocks(
        lax.dot_general(
            grad_logits, student_emb, (((0,), (0,)), ((), ())), preferred_element_type=jnp.float32
        )
        / student_temp,
        "dp",
    )
    return (grad_prototypes, grad_student)


def solution(mesh):
    in_specs = (P("dp", None), P("dp", None), P(("dp", "proto"), None))
    out_specs = (P(("dp", "proto"), None), P("dp", None))
    return jax.shard_map(
        per_device, mesh=mesh, in_specs=in_specs, out_specs=out_specs, check_vma=False
    )
```

```python
import math

import jax
import jax.numpy as jnp
from jax import lax
from jax.sharding import PartitionSpec as P

ITERS = 3


teacher_temp = 0.07
student_temp = 0.1


def swap(x, axis, k):
    n = lax.axis_size(axis)
    return lax.ppermute(x, axis, [(i, i ^ (1 << k)) for i in range(n)])


def bits(axis):
    return int(math.log2(lax.axis_size(axis)))


GATHER_ORDER = ((6, 3, 5, 2, 4, 1, 0), (3, 6, 2, 5, 1, 4, 0))


def core_swap(x, axis, step, orders):
    n = lax.axis_size(axis)
    pairs = [(i, i ^ (1 << orders[i & 1][step])) for i in range(n)]
    return lax.ppermute(x, axis, pairs)


def core_bit(me, step, orders):
    k = jnp.where((me & 1) == 0, orders[0][step], orders[1][step])
    return (me >> k) & 1


def swap_halves(x):
    shape = (2,) * 6 + (x.shape[0] // 64,) + x.shape[1:]
    dims = (1, 0, 3, 2, 5, 4) + tuple(range(6, len(shape)))
    return x.reshape(shape).transpose(dims).reshape(x.shape)


def gather_blocks(x, axis):
    me = lax.axis_index(axis)
    steps = len(GATHER_ORDER[0])
    for step in range(steps):
        bit = core_bit(me, step, GATHER_ORDER)
        other = core_swap(x, axis, step, GATHER_ORDER)
        if step == steps - 1:
            other = swap_halves(other)
        buf = jnp.zeros((2,) + x.shape, x.dtype)
        buf = lax.dynamic_update_index_in_dim(buf, x, bit, 0)
        buf = lax.dynamic_update_index_in_dim(buf, other, 1 - bit, 0)
        x = buf.reshape((-1,) + x.shape[1:])
    return x


def scatter_blocks(x, axis):
    me = lax.axis_index(axis)
    orders = tuple(tuple(reversed(o)) for o in GATHER_ORDER)
    for step in range(len(orders[0])):
        bit = core_bit(me, step, orders)
        x = x.reshape((2, x.shape[0] // 2) + x.shape[1:])
        keep = lax.dynamic_index_in_dim(x, bit, 0, keepdims=False)
        send = lax.dynamic_index_in_dim(x, 1 - bit, 0, keepdims=False)
        other = core_swap(send, axis, step, orders)
        if step == 0:
            other = swap_halves(other)
        x = keep + other
    return x


def sum_over(x, axis):
    for k in range(bits(axis)):
        x = x + swap(x, axis, k)
    return x


def column_sum(x, axis):
    for k in range(bits(axis)):
        other = swap(x, axis, k)
        if k == 0:
            other = jax.vmap(swap_halves)(other.reshape(2, -1, 1)).reshape(x.shape)
        x = x + other
    return x


def contract_rows(left, right):
    return lax.dot_general(
        left, right, (((1,), (1,)), ((), ())), preferred_element_type=jnp.float32
    )


def combine_stats(first, second):
    teacher_top = jnp.maximum(first[0], second[0])
    student_top = jnp.maximum(first[1], second[1])
    total = first[2] * jnp.exp(first[1] - student_top) + second[2] * jnp.exp(
        second[1] - student_top
    )
    return jnp.stack([teacher_top, student_top, total])


def per_device(teacher_emb, student_emb, prototypes):
    copies = gather_blocks(prototypes.astype(jnp.bfloat16), "dp")
    rows_here = teacher_emb.shape[0]
    width = teacher_emb.shape[1]
    block = rows_here
    count_blocks = rows_here // block

    def teacher_block(emb):
        logits = contract_rows(emb, copies)
        top = jnp.max(logits, axis=1)
        return (jnp.exp((logits - top[:, None]) / teacher_temp), top)

    base_local, teacher_local = lax.map(
        teacher_block, teacher_emb.reshape(count_blocks, block, width)
    )
    base_local = base_local.reshape(rows_here, -1)
    teacher_local = teacher_local.reshape(rows_here)

    def student_stats(emb):
        logits = contract_rows(emb, copies) / student_temp
        top = jnp.max(logits, axis=1)
        return (top, jnp.sum(jnp.exp(logits - top[:, None]), axis=1))

    student_local, total_local = lax.map(
        student_stats, student_emb.reshape(count_blocks, block, width)
    )
    student_local = student_local.reshape(rows_here)
    total_local = total_local.reshape(rows_here)
    teacher_top = lax.pmax(teacher_local, "proto")
    student_pair = jnp.stack([student_local, total_local])
    for k in range(bits("proto")):
        other = swap(student_pair, "proto", k)
        top = jnp.maximum(student_pair[0], other[0])
        student_pair = jnp.stack(
            [top, student_pair[1] * jnp.exp(student_pair[0] - top) + other[1] * jnp.exp(other[0] - top)]
        )
    student_top, total = student_pair[0], student_pair[1]
    shift = jnp.exp((teacher_local - teacher_top) / teacher_temp)
    row_scale = jnp.ones((rows_here,), jnp.float32)
    col_scale = jnp.ones((base_local.shape[1],), jnp.float32)
    for step in range(ITERS):
        partial_cols = jnp.sum((row_scale * shift)[:, None] * base_local, axis=0)
        col_scale = 1.0 / column_sum(partial_cols, "dp")
        partial_rows = shift * jnp.sum(base_local * col_scale[None, :], axis=1)
        row_scale = 1.0 / lax.psum(partial_rows, "proto")
    row_factor = row_scale * shift
    student_factor = jnp.exp(student_local - student_top) / total

    def gradient_block(items):
        emb, plan, factor, local_top, soft_factor = items
        logits = contract_rows(emb, copies) / student_temp
        probs = jnp.exp(logits - local_top[:, None]) * soft_factor[:, None]
        targets = factor[:, None] * plan * col_scale[None, :]
        grads = (probs - targets).astype(jnp.bfloat16)
        return (grads, jnp.dot(grads, copies, preferred_element_type=jnp.float32) / student_temp)

    grad_logits, student_terms = lax.map(
        gradient_block,
        (
            student_emb.reshape(count_blocks, block, width),
            base_local.reshape(count_blocks, block, -1),
            row_factor.reshape(count_blocks, block),
            student_local.reshape(count_blocks, block),
            student_factor.reshape(count_blocks, block),
        ),
    )
    grad_logits = grad_logits.reshape(rows_here, -1)
    grad_student = sum_over(student_terms.reshape(rows_here, width), "proto")
    grad_prototypes = scatter_blocks(
        lax.dot_general(
            grad_logits, student_emb, (((0,), (0,)), ((), ())), preferred_element_type=jnp.float32
        )
        / student_temp,
        "dp",
    )
    return (grad_prototypes, grad_student)


def solution(mesh):
    in_specs = (P("dp", None), P("dp", None), P(("dp", "proto"), None))
    out_specs = (P(("dp", "proto"), None), P("dp", None))
    return jax.shard_map(
        per_device, mesh=mesh, in_specs=in_specs, out_specs=out_specs, check_vma=False
    )
```

```python
import math

import jax
import jax.numpy as jnp
from jax import lax
from jax.sharding import PartitionSpec as P

ITERS = 3


teacher_temp = 0.07
student_temp = 0.1


def swap(x, axis, k):
    n = lax.axis_size(axis)
    return lax.ppermute(x, axis, [(i, i ^ (1 << k)) for i in range(n)])


def bits(axis):
    return int(math.log2(lax.axis_size(axis)))


GATHER_ORDER = ((6, 3, 5, 2, 4, 1, 0), (3, 6, 2, 5, 1, 4, 0))


def core_swap(x, axis, step, orders):
    n = lax.axis_size(axis)
    pairs = [(i, i ^ (1 << orders[i & 1][step])) for i in range(n)]
    return lax.ppermute(x, axis, pairs)


def core_bit(me, step, orders):
    k = jnp.where((me & 1) == 0, orders[0][step], orders[1][step])
    return (me >> k) & 1


def swap_halves(x):
    shape = (2,) * 6 + (x.shape[0] // 64,) + x.shape[1:]
    dims = (1, 0, 3, 2, 5, 4) + tuple(range(6, len(shape)))
    return x.reshape(shape).transpose(dims).reshape(x.shape)


def gather_blocks(x, axis):
    me = lax.axis_index(axis)
    steps = len(GATHER_ORDER[0])
    for step in range(steps):
        bit = core_bit(me, step, GATHER_ORDER)
        other = core_swap(x, axis, step, GATHER_ORDER)
        if step == steps - 1:
            other = swap_halves(other)
        buf = jnp.zeros((2,) + x.shape, x.dtype)
        buf = lax.dynamic_update_index_in_dim(buf, x, bit, 0)
        buf = lax.dynamic_update_index_in_dim(buf, other, 1 - bit, 0)
        x = buf.reshape((-1,) + x.shape[1:])
    return x


def scatter_blocks(x, axis):
    me = lax.axis_index(axis)
    orders = tuple(tuple(reversed(o)) for o in GATHER_ORDER)
    for step in range(len(orders[0])):
        bit = core_bit(me, step, orders)
        x = x.reshape((2, x.shape[0] // 2) + x.shape[1:])
        keep = lax.dynamic_index_in_dim(x, bit, 0, keepdims=False)
        send = lax.dynamic_index_in_dim(x, 1 - bit, 0, keepdims=False)
        other = core_swap(send, axis, step, orders)
        if step == 0:
            other = swap_halves(other)
        x = keep + other
    return x


def sum_over(x, axis):
    for k in range(bits(axis)):
        x = x + swap(x, axis, k)
    return x


def column_sum(x, axis):
    for k in range(bits(axis)):
        other = swap(x, axis, k)
        if k == 0:
            other = jax.vmap(swap_halves)(other.reshape(2, -1, 1)).reshape(x.shape)
        x = x + other
    return x


def contract_rows(left, right):
    return lax.dot_general(
        left, right, (((1,), (1,)), ((), ())), preferred_element_type=jnp.float32
    )


def combine_stats(first, second):
    teacher_top = jnp.maximum(first[0], second[0])
    student_top = jnp.maximum(first[1], second[1])
    total = first[2] * jnp.exp(first[1] - student_top) + second[2] * jnp.exp(
        second[1] - student_top
    )
    return jnp.stack([teacher_top, student_top, total])


def per_device(teacher_emb, student_emb, prototypes):
    copies = gather_blocks(prototypes.astype(jnp.bfloat16), "dp")
    rows_here = teacher_emb.shape[0]
    width = teacher_emb.shape[1]
    block = rows_here
    count_blocks = rows_here // block

    def teacher_block(emb):
        logits = contract_rows(emb, copies)
        top = jnp.max(logits, axis=1)
        return (jnp.exp((logits - top[:, None]) / teacher_temp), top)

    base_local, teacher_local = lax.map(
        teacher_block, teacher_emb.reshape(count_blocks, block, width)
    )
    base_local = base_local.reshape(rows_here, -1)
    teacher_local = teacher_local.reshape(rows_here)

    def student_stats(emb):
        logits = contract_rows(emb, copies) / student_temp
        top = jnp.max(logits, axis=1)
        expo = jnp.exp(logits - top[:, None])
        return (top, jnp.sum(expo, axis=1), expo)

    student_local, total_local, student_expo = lax.map(
        student_stats, student_emb.reshape(count_blocks, block, width)
    )
    student_local = student_local.reshape(rows_here)
    total_local = total_local.reshape(rows_here)
    every = lax.all_gather(
        jnp.stack([teacher_local, student_local, total_local]), "proto", axis=0, tiled=False
    )
    stats = every[0]
    for j in range(1, every.shape[0]):
        stats = combine_stats(stats, every[j])
    teacher_top, student_top, total = stats[0], stats[1], stats[2]
    shift = jnp.exp((teacher_local - teacher_top) / teacher_temp)
    row_scale = jnp.ones((rows_here,), jnp.float32)
    col_scale = jnp.ones((base_local.shape[1],), jnp.float32)
    for step in range(ITERS):
        partial_cols = jnp.sum((row_scale * shift)[:, None] * base_local, axis=0)
        col_scale = 1.0 / column_sum(partial_cols, "dp")
        partial_rows = shift * jnp.sum(base_local * col_scale[None, :], axis=1)
        row_scale = 1.0 / lax.psum(partial_rows, "proto")
    row_factor = row_scale * shift
    student_factor = jnp.exp(student_local - student_top) / total

    def gradient_block(items):
        expo, plan, factor, soft_factor = items
        probs = expo * soft_factor[:, None]
        targets = factor[:, None] * plan * col_scale[None, :]
        grads = (probs - targets).astype(jnp.bfloat16)
        return (grads, jnp.dot(grads, copies, preferred_element_type=jnp.float32) / student_temp)

    grad_logits, student_terms = lax.map(
        gradient_block,
        (
            student_expo.reshape(count_blocks, block, -1),
            base_local.reshape(count_blocks, block, -1),
            row_factor.reshape(count_blocks, block),
            student_factor.reshape(count_blocks, block),
        ),
    )
    grad_logits = grad_logits.reshape(rows_here, -1)
    grad_student = sum_over(student_terms.reshape(rows_here, width), "proto")
    grad_prototypes = scatter_blocks(
        lax.dot_general(
            grad_logits, student_emb, (((0,), (0,)), ((), ())), preferred_element_type=jnp.float32
        )
        / student_temp,
        "dp",
    )
    return (grad_prototypes, grad_student)


def solution(mesh):
    in_specs = (P("dp", None), P("dp", None), P(("dp", "proto"), None))
    out_specs = (P(("dp", "proto"), None), P("dp", None))
    return jax.shard_map(
        per_device, mesh=mesh, in_specs=in_specs, out_specs=out_specs, check_vma=False
    )
```
